32 devices in a mesh: tm: 8 (over z, core), space: 4 (over y, x).
Axes of the slice: x: 2, y: 2, z: 4, core: 2. Of those that a mesh axis runs over, the one named last changes fastest.
Arguments:
- volumes: float32 [8, 64, 512, 128], P('tm', 'space'), may hold values from -12 to 12
Outputs:
- corrected: float32 [8, 64, 512, 128], P('tm', 'space')
- shifts: float32 [8, 3], P('tm')
The draws below stay inside these ranges and needn't reach their ends.
All inputs are finite; a program needn't handle non-finite values.
Results may differ from the reference program's by a relative error of at most 0.0003.
Values sent between devices are 32-bit elements; how exact they have to be, the bound alone decides.
No kernel may reach another device: no remote copies, remote signals or barrier semaphores. Data moves between devices by JAX's collectives and lax.ppermute only.
A program may use at most 128 MiB of HBM per device.

```python
import math
import jax
import jax.numpy as jnp
from jax import lax

X = 512
Y = 128
Z = 64
ITERS = 2
TIMES = 8


def draw_volumes(key, part):
    structure = jax.random.normal(jax.random.fold_in(key, 11), (Z, X, Y), jnp.float32)
    noise_field = jax.random.normal(jax.random.fold_in(key, 12), (TIMES, Z, X, Y), jnp.float32)
    drift_steps = jax.random.randint(jax.random.fold_in(key, 13), (TIMES, 3), -2, 3)
    jitter = jax.random.uniform(jax.random.fold_in(key, 14), (TIMES,), jnp.float32, 0.6, 1.4)
    ramp_pos = jnp.arange(TIMES, dtype=jnp.float32) / max(TIMES - 1, 1)
    bright = jnp.exp(-math.log(3.0) * ramp_pos) * jitter

    def place_one(offsets):
        return jnp.roll(structure, (offsets[0], offsets[1], offsets[2]), axis=(0, 1, 2))
    rolled = jax.vmap(place_one)(drift_steps)
    volumes = bright[:, None, None, None] * rolled + 0.5 * noise_field
    return jnp.clip(volumes, -12.0, 12.0)


def setup_inputs(seed: int = 0) -> dict:
    seeds = jax.random.split(jax.random.key(seed), 2)
    return {
        "volumes": draw_volumes(jax.random.fold_in(seeds[1], 71), 0),
    }


sharpness = 256.0
floor_share = 0.05


def signed_freq(length):
    indices = jnp.arange(length, dtype=jnp.int32)
    wrapped = jnp.where(indices < length // 2, indices, indices - length)
    return jnp.where(indices == length // 2, 0, wrapped).astype(jnp.float32)


def centred(length):
    indices = jnp.arange(length, dtype=jnp.int32)
    return ((indices + length // 2) % length - length // 2).astype(jnp.float32)


def register(spectrum, template):
    product = spectrum * jnp.conj(template)
    magnitude = jnp.abs(product)
    whitened = product / jnp.maximum(magnitude, floor_share * (Z * X * Y))
    correlation = jnp.real(jnp.fft.ifftn(whitened))
    scores = sharpness * correlation
    weights = jnp.exp(scores - jnp.max(scores))
    weight_sum = jnp.sum(weights)
    moment_z = jnp.sum(jnp.sum(weights, axis=(1, 2)) * centred(Z))
    moment_x = jnp.sum(jnp.sum(weights, axis=(0, 2)) * centred(X))
    moment_y = jnp.sum(jnp.sum(weights, axis=(0, 1)) * centred(Y))
    shifts = jnp.stack([moment_z, moment_x, moment_y]) / weight_sum
    phases = (2.0 * math.pi) * (signed_freq(Z)[:, None, None] * (shifts[0] / Z)
                                + signed_freq(X)[None, :, None] * (shifts[1] / X)
                                + signed_freq(Y)[None, None, :] * (shifts[2] / Y))
    shifted = spectrum * (jnp.cos(phases) + 1j * jnp.sin(phases))
    return shifts, shifted


def reference(volumes):
    spectra = jnp.fft.fftn(volumes, axes=(1, 2, 3))
    template = jnp.mean(spectra, axis=0)
    for iteration in range(ITERS):
        shifts, shifted = lax.map(lambda spectrum: register(spectrum, template), spectra)
        template = jnp.mean(shifted, axis=0)
    corrected = jnp.real(jnp.fft.ifftn(shifted, axes=(1, 2, 3))).astype(jnp.float32)
    return corrected, shifts.astype(jnp.float32)
```

```python
import math

import jax
import jax.numpy as jnp
from jax import lax
from jax.sharding import PartitionSpec as P

X = 512
Y = 128
Z = 64
ITERS = 2
HALF = X // 2

precise = lax.Precision.HIGHEST
sharpness = 256.0
floor_share = 0.05


def angles(rows, cols, length):
    products = rows[:, None] * cols[None, :] % length
    return products.astype(jnp.float32) * (2.0 * math.pi / length)


def x_tables():
    k = jnp.arange(HALF, dtype=jnp.int32)
    n = jnp.arange(X, dtype=jnp.int32)
    theta = angles(k, n, X)
    cos = jnp.cos(theta)
    sin = jnp.sin(theta)
    alt = jnp.where(n % 2 == 0, 1.0, -1.0).astype(jnp.float32)[None, :]
    first = (k == 0)[:, None]
    fwd = jnp.concatenate([cos, jnp.where(first, alt, -sin)], axis=0)
    norming = 1.0 / (X * Y * Z)
    inv_re = jnp.where(first, 1.0, 2.0 * cos) * norming
    inv_im = jnp.where(first, alt, -2.0 * sin) * norming
    inv = jnp.concatenate([inv_re, inv_im], axis=0).T
    return fwd, inv


def y_tables():
    k = jnp.arange(Y, dtype=jnp.int32)
    theta = angles(k, k, Y)
    return jnp.cos(theta), jnp.sin(theta)


def z_tables():
    k = jnp.arange(Z, dtype=jnp.int32)
    theta = angles(k, k, Z)
    c = jnp.cos(theta)
    s = jnp.sin(theta)
    fwd = jnp.stack([jnp.stack([c, s], axis=-1), jnp.stack([-s, c], axis=-1)], axis=1)
    inv = jnp.stack([jnp.stack([c, -s], axis=-1), jnp.stack([s, c], axis=-1)], axis=1)
    return fwd.reshape(2 * Z, 2 * Z), inv.reshape(2 * Z, 2 * Z)


def signed_freq(indices, length):
    wrapped = jnp.where(indices < length // 2, indices, indices - length)
    return jnp.where(indices == length // 2, 0, wrapped).astype(jnp.float32)


def centred(indices, length):
    return ((indices + length // 2) % length - length // 2).astype(jnp.float32)


def dot_y(data, table):
    return jnp.einsum("...y,yk->...k", data, table, precision=precise)


def mix_z(table, data):
    v, nz, two, nk, ny = data.shape
    flat = data.reshape(v, nz * two, nk * ny)
    out = jnp.einsum("pq,vqr->vpr", table, flat, precision=precise)
    return out.reshape(v, nz, two, nk, ny)


def forward(volume, tables):
    x_fwd, _, cos_y, sin_y, z_fwd, _ = tables
    v, nz = volume.shape[0], volume.shape[1]
    a = jnp.einsum("qn,vzny->vzqy", x_fwd, volume, precision=precise)
    a = a.reshape(v, nz, 2, HALF, Y)
    re, im = a[:, :, 0], a[:, :, 1]
    a = jnp.stack(
        [dot_y(re, cos_y) + dot_y(im, sin_y), dot_y(im, cos_y) - dot_y(re, sin_y)], axis=2
    )
    a = lax.all_to_all(a, "space", split_axis=3, concat_axis=1, tiled=True)
    return mix_z(z_fwd, a)


def mirror(col):
    return jnp.roll(jnp.flip(col, axis=(1, 3)), 1, axis=(1, 3))


def unpack(spectrum, first):
    col = spectrum[:, :, :, 0, :]
    mir = mirror(col)
    c_re, c_im = col[:, :, 0], col[:, :, 1]
    m_re, m_im = mir[:, :, 0], mir[:, :, 1]
    low = jnp.stack([(c_re + m_re) * 0.5, (c_im - m_im) * 0.5], axis=2)
    nyq = jnp.stack([(c_im + m_im) * 0.5, (m_re - c_re) * 0.5], axis=2)
    spectrum = spectrum.at[:, :, :, 0, :].set(jnp.where(first, low, col))
    return spectrum, jnp.where(first, nyq, 0.0)


def pack(spectrum, nyq):
    col = spectrum[:, :, :, 0, :]
    packed = jnp.stack([col[:, :, 0] - nyq[:, :, 1], col[:, :, 1] + nyq[:, :, 0]], axis=2)
    return spectrum.at[:, :, :, 0, :].set(packed)


def inverse(spectrum, nyq, tables):
    _, x_inv, cos_y, sin_y, _, z_inv = tables
    a = mix_z(z_inv, pack(spectrum, nyq))
    re, im = a[:, :, 0], a[:, :, 1]
    a = jnp.stack(
        [dot_y(re, cos_y) - dot_y(im, sin_y), dot_y(re, sin_y) + dot_y(im, cos_y)], axis=2
    )
    a = lax.all_to_all(a, "space", split_axis=1, concat_axis=3, tiled=True)
    v, nz = a.shape[0], a.shape[1]
    a = a.reshape(v, nz, 2 * HALF, Y)
    return jnp.einsum("nq,vzqy->vzny", x_inv, a, precision=precise)


def whiten(spec, tmpl):
    s_re, s_im = spec[:, :, 0], spec[:, :, 1]
    t_re, t_im = tmpl[:, :, 0], tmpl[:, :, 1]
    prod_re = s_re * t_re + s_im * t_im
    prod_im = s_im * t_re - s_re * t_im
    divisor = jnp.maximum(
        jnp.sqrt(prod_re * prod_re + prod_im * prod_im), floor_share * (X * Y * Z)
    )
    return jnp.stack([prod_re / divisor, prod_im / divisor], axis=2)


def weight_moments(weights, coords):
    coord_z, coord_x, coord_y = coords
    weight_sum = jnp.sum(weights, axis=(1, 2, 3))
    moment_z = jnp.sum(jnp.sum(weights, axis=(2, 3)) * coord_z[None, :], axis=1)
    moment_x = jnp.sum(jnp.sum(weights, axis=(1, 3)) * coord_x[None, :], axis=1)
    moment_y = jnp.sum(jnp.sum(weights, axis=(1, 2)) * coord_y[None, :], axis=1)
    return (weight_sum, jnp.stack([moment_z, moment_x, moment_y], axis=1))


def centroid(scores, coords):
    local_top = jnp.max(scores, axis=(1, 2, 3))
    top_score = lax.pmax(local_top, "space")
    weights = jnp.exp(scores - top_score[:, None, None, None])
    weight_sum, moments = weight_moments(weights, coords)
    weight_sum, moments = lax.psum((weight_sum, moments), "space")
    return moments / weight_sum[:, None]


def unit(phase):
    return jnp.cos(phase), jnp.sin(phase)


def cmul(a, b):
    return (a[0] * b[0] - a[1] * b[1], a[0] * b[1] + a[1] * b[0])


def apply_ramp(spec, nyq, shifts, freq_z, freq_x, freq_y):
    ez = unit(2.0 * math.pi * freq_z[None, :] * (shifts[:, 0] / Z)[:, None])
    ex = unit(2.0 * math.pi * freq_x[None, :] * (shifts[:, 1] / X)[:, None])
    ey = unit(2.0 * math.pi * freq_y[None, :] * (shifts[:, 2] / Y)[:, None])
    exy = cmul((ex[0][:, :, None], ex[1][:, :, None]), (ey[0][:, None, :], ey[1][:, None, :]))
    ezy = cmul((ez[0][:, :, None], ez[1][:, :, None]), (ey[0][:, None, :], ey[1][:, None, :]))
    e = cmul((ez[0][:, :, None, None], ez[1][:, :, None, None]), (exy[0][:, None], exy[1][:, None]))
    main = cmul((spec[:, :, 0], spec[:, :, 1]), e)
    edge = cmul((nyq[:, :, 0], nyq[:, :, 1]), ezy)
    return jnp.stack(main, axis=2), jnp.stack(edge, axis=2)


def body(volumes):
    position = lax.axis_index("space")
    first = position == 0
    slab_depth = volumes.shape[1]
    pencil = HALF // lax.axis_size("space")
    frames = volumes.shape[0] * lax.axis_size("tm")
    tables = x_tables() + y_tables() + z_tables()
    z_index = position * slab_depth + jnp.arange(slab_depth, dtype=jnp.int32)
    x_index = position * pencil + jnp.arange(pencil, dtype=jnp.int32)
    coords = (
        centred(z_index, Z),
        centred(jnp.arange(X, dtype=jnp.int32), X),
        centred(jnp.arange(Y, dtype=jnp.int32), Y),
    )
    freq_z = signed_freq(jnp.arange(Z, dtype=jnp.int32), Z)
    freq_x = x_index.astype(jnp.float32)
    freq_y = signed_freq(jnp.arange(Y, dtype=jnp.int32), Y)
    spec, spec_nyq = unpack(forward(volumes, tables), first)
    shifted, shifted_nyq = spec, spec_nyq
    for iteration in range(ITERS):
        summed, summed_nyq = lax.psum((jnp.sum(shifted, axis=0), jnp.sum(shifted_nyq, axis=0)), "tm")
        tmpl = summed[None] / frames
        tmpl_nyq = summed_nyq[None] / frames
        white = whiten(spec, tmpl)
        white_nyq = whiten(spec_nyq, tmpl_nyq)
        correlation = inverse(white, white_nyq, tables)
        shifts = centroid(sharpness * correlation, coords)
        shifted, shifted_nyq = apply_ramp(spec, spec_nyq, shifts, freq_z, freq_x, freq_y)
    corrected = inverse(shifted, shifted_nyq, tables)
    return (corrected, shifts)


def solution(mesh):
    in_specs = (P("tm", "space", None, None),)
    out_specs = (P("tm", "space", None, None), P("tm", None))
    return jax.shard_map(body, mesh=mesh, in_specs=in_specs, out_specs=out_specs, check_vma=False)
```

```python
import math

import jax
import jax.numpy as jnp
from jax import lax
from jax.sharding import PartitionSpec as P

X = 512
Y = 128
Z = 64
ITERS = 2
HALF = X // 2

precise = lax.Precision.HIGHEST
sharpness = 256.0
floor_share = 0.05


def angles(rows, cols, length):
    products = rows[:, None] * cols[None, :] % length
    return products.astype(jnp.float32) * (2.0 * math.pi / length)


def x_tables():
    k = jnp.arange(HALF, dtype=jnp.int32)
    n = jnp.arange(X, dtype=jnp.int32)
    theta = angles(k, n, X)
    cos = jnp.cos(theta)
    sin = jnp.sin(theta)
    alt = jnp.where(n % 2 == 0, 1.0, -1.0).astype(jnp.float32)[None, :]
    first = (k == 0)[:, None]
    fwd = jnp.concatenate([cos, jnp.where(first, alt, -sin)], axis=0)
    norming = 1.0 / (X * Y * Z)
    inv_re = jnp.where(first, 1.0, 2.0 * cos) * norming
    inv_im = jnp.where(first, alt, -2.0 * sin) * norming
    inv = jnp.concatenate([inv_re, inv_im], axis=0).T
    return fwd, inv


def y_tables():
    k = jnp.arange(Y, dtype=jnp.int32)
    theta = angles(k, k, Y)
    return jnp.cos(theta), jnp.sin(theta)


def z_tables():
    k = jnp.arange(Z, dtype=jnp.int32)
    theta = angles(k, k, Z)
    c = jnp.cos(theta)
    s = jnp.sin(theta)
    fwd = jnp.stack([jnp.stack([c, s], axis=-1), jnp.stack([-s, c], axis=-1)], axis=1)
    inv = jnp.stack([jnp.stack([c, -s], axis=-1), jnp.stack([s, c], axis=-1)], axis=1)
    return fwd.reshape(2 * Z, 2 * Z), inv.reshape(2 * Z, 2 * Z)


def signed_freq(indices, length):
    wrapped = jnp.where(indices < length // 2, indices, indices - length)
    return jnp.where(indices == length // 2, 0, wrapped).astype(jnp.float32)


def centred(indices, length):
    return ((indices + length // 2) % length - length // 2).astype(jnp.float32)


def dot_y(data, table, precision=precise):
    return jnp.einsum("...y,yk->...k", data, table, precision=precision)


def mix_z(table, data, precision=precise):
    v, nz, two, nk, ny = data.shape
    flat = data.reshape(v, nz * two, nk * ny)
    out = jnp.einsum("pq,vqr->vpr", table, flat, precision=precision)
    return out.reshape(v, nz, two, nk, ny)


def forward(volume, tables):
    x_fwd, _, cos_y, sin_y, z_fwd, _ = tables
    v, nz = volume.shape[0], volume.shape[1]
    a = jnp.einsum("qn,vzny->vzqy", x_fwd, volume, precision=precise)
    a = a.reshape(v, nz, 2, HALF, Y)
    re, im = a[:, :, 0], a[:, :, 1]
    a = jnp.stack(
        [dot_y(re, cos_y) + dot_y(im, sin_y), dot_y(im, cos_y) - dot_y(re, sin_y)], axis=2
    )
    a = lax.all_to_all(a, "space", split_axis=3, concat_axis=1, tiled=True)
    return mix_z(z_fwd, a)


def mirror(col):
    return jnp.roll(jnp.flip(col, axis=(1, 3)), 1, axis=(1, 3))


def unpack(spectrum, first):
    col = spectrum[:, :, :, 0, :]
    mir = mirror(col)
    c_re, c_im = col[:, :, 0], col[:, :, 1]
    m_re, m_im = mir[:, :, 0], mir[:, :, 1]
    low = jnp.stack([(c_re + m_re) * 0.5, (c_im - m_im) * 0.5], axis=2)
    nyq = jnp.stack([(c_im + m_im) * 0.5, (m_re - c_re) * 0.5], axis=2)
    spectrum = spectrum.at[:, :, :, 0, :].set(jnp.where(first, low, col))
    return spectrum, jnp.where(first, nyq, 0.0)


def pack(spectrum, nyq):
    col = spectrum[:, :, :, 0, :]
    packed = jnp.stack([col[:, :, 0] - nyq[:, :, 1], col[:, :, 1] + nyq[:, :, 0]], axis=2)
    return spectrum.at[:, :, :, 0, :].set(packed)


def inverse(spectrum, nyq, tables, precision=precise):
    _, x_inv, cos_y, sin_y, _, z_inv = tables
    a = mix_z(z_inv, pack(spectrum, nyq), precision)
    re, im = a[:, :, 0], a[:, :, 1]
    a = jnp.stack(
        [
            dot_y(re, cos_y, precision) - dot_y(im, sin_y, precision),
            dot_y(re, sin_y, precision) + dot_y(im, cos_y, precision),
        ],
        axis=2,
    )
    a = lax.all_to_all(a, "space", split_axis=1, concat_axis=3, tiled=True)
    v, nz = a.shape[0], a.shape[1]
    a = a.reshape(v, nz, 2 * HALF, Y)
    return jnp.einsum("nq,vzqy->vzny", x_inv, a, precision=precision)


def whiten(spec, tmpl):
    s_re, s_im = spec[:, :, 0], spec[:, :, 1]
    t_re, t_im = tmpl[:, :, 0], tmpl[:, :, 1]
    prod_re = s_re * t_re + s_im * t_im
    prod_im = s_im * t_re - s_re * t_im
    divisor = jnp.maximum(
        jnp.sqrt(prod_re * prod_re + prod_im * prod_im), floor_share * (X * Y * Z)
    )
    return jnp.stack([prod_re / divisor, prod_im / divisor], axis=2)


def weight_moments(weights, coords):
    coord_z, coord_x, coord_y = coords
    weight_sum = jnp.sum(weights, axis=(1, 2, 3))
    moment_z = jnp.sum(jnp.sum(weights, axis=(2, 3)) * coord_z[None, :], axis=1)
    moment_x = jnp.sum(jnp.sum(weights, axis=(1, 3)) * coord_x[None, :], axis=1)
    moment_y = jnp.sum(jnp.sum(weights, axis=(1, 2)) * coord_y[None, :], axis=1)
    return (weight_sum, jnp.stack([moment_z, moment_x, moment_y], axis=1))


def centroid(scores, coords):
    local_top = jnp.max(scores, axis=(1, 2, 3))
    weights = jnp.exp(scores - local_top[:, None, None, None])
    weight_sum, moments = weight_moments(weights, coords)
    local = jnp.concatenate([local_top[:, None], weight_sum[:, None], moments], axis=1)
    gathered = lax.all_gather(local, "space")
    scale = jnp.exp(gathered[:, :, 0] - jnp.max(gathered[:, :, 0], axis=0)[None, :])
    totals = jnp.sum(gathered[:, :, 1:] * scale[:, :, None], axis=0)
    return totals[:, 1:] / totals[:, 0:1]


def unit(phase):
    return jnp.cos(phase), jnp.sin(phase)


def cmul(a, b):
    return (a[0] * b[0] - a[1] * b[1], a[0] * b[1] + a[1] * b[0])


def apply_ramp(spec, nyq, shifts, freq_z, freq_x, freq_y):
    ez = unit(2.0 * math.pi * freq_z[None, :] * (shifts[:, 0] / Z)[:, None])
    ex = unit(2.0 * math.pi * freq_x[None, :] * (shifts[:, 1] / X)[:, None])
    ey = unit(2.0 * math.pi * freq_y[None, :] * (shifts[:, 2] / Y)[:, None])
    exy = cmul((ex[0][:, :, None], ex[1][:, :, None]), (ey[0][:, None, :], ey[1][:, None, :]))
    ezy = cmul((ez[0][:, :, None], ez[1][:, :, None]), (ey[0][:, None, :], ey[1][:, None, :]))
    e = cmul((ez[0][:, :, None, None], ez[1][:, :, None, None]), (exy[0][:, None], exy[1][:, None]))
    main = cmul((spec[:, :, 0], spec[:, :, 1]), e)
    edge = cmul((nyq[:, :, 0], nyq[:, :, 1]), ezy)
    return jnp.stack(main, axis=2), jnp.stack(edge, axis=2)


def body(volumes):
    position = lax.axis_index("space")
    first = position == 0
    slab_depth = volumes.shape[1]
    pencil = HALF // lax.axis_size("space")
    frames = volumes.shape[0] * lax.axis_size("tm")
    tables = x_tables() + y_tables() + z_tables()
    z_index = position * slab_depth + jnp.arange(slab_depth, dtype=jnp.int32)
    x_index = position * pencil + jnp.arange(pencil, dtype=jnp.int32)
    coords = (
        centred(z_index, Z),
        centred(jnp.arange(X, dtype=jnp.int32), X),
        centred(jnp.arange(Y, dtype=jnp.int32), Y),
    )
    freq_z = signed_freq(jnp.arange(Z, dtype=jnp.int32), Z)
    freq_x = x_index.astype(jnp.float32)
    freq_y = signed_freq(jnp.arange(Y, dtype=jnp.int32), Y)
    spec, spec_nyq = unpack(forward(volumes, tables), first)
    shifted, shifted_nyq = spec, spec_nyq
    for iteration in range(ITERS):
        summed, summed_nyq = lax.psum((jnp.sum(shifted, axis=0), jnp.sum(shifted_nyq, axis=0)), "tm")
        tmpl = summed[None] / frames
        tmpl_nyq = summed_nyq[None] / frames
        white = whiten(spec, tmpl)
        white_nyq = whiten(spec_nyq, tmpl_nyq)
        correlation = inverse(white, white_nyq, tables)
        shifts = centroid(sharpness * correlation, coords)
        shifted, shifted_nyq = apply_ramp(spec, spec_nyq, shifts, freq_z, freq_x, freq_y)
    corrected = inverse(shifted, shifted_nyq, tables, lax.Precision.HIGH)
    return (corrected, shifts)


def solution(mesh):
    in_specs = (P("tm", "space", None, None),)
    out_specs = (P("tm", "space", None, None), P("tm", None))
    return jax.shard_map(body, mesh=mesh, in_specs=in_specs, out_specs=out_specs, check_vma=False)
```
